256 devices in a mesh: row: 32 (over x, z), col: 8 (over y, core).
Axes of the slice: x: 4, y: 4, z: 8, core: 2. Of those that a mesh axis runs over, the one named last changes fastest.
Arguments:
- points: float32 [16384, 256], P('row'), may hold values from -6 to 6
- nugget: float32 [16384], P('row'), may hold values from 0.5 to 2
- weights: float32 [256], replicated, may hold values from 0.0005 to 0.005
- band_start: int32 [32], replicated, may hold values from 0 to 30, as said below
Outputs:
- factored: float32 [32, 4, 8, 512, 512], P('row', None, 'col')
The draws below stay inside these ranges and needn't reach their ends.
Inputs may be any that keep to these rules, and one draw needn't show every extreme that they name: band_start[i] <= i - 1 for every i >= 1, band_start[0] = 0; band_start[17] = 0; the last tile row has band_start = 30.
All inputs are finite; a program needn't handle non-finite values.
Results may differ from the reference program's by a relative error of at most 0.0003.
Values sent between devices are 32-bit elements; how exact they have to be, the bound alone decides.
No kernel may reach another device: no remote copies, remote signals or barrier semaphores. Data moves between devices by JAX's collectives and lax.ppermute only.
A program may use at most 128 MiB of HBM per device.

```python
import math
import jax
import jax.numpy as jnp
from jax import lax

TILE = 512
COV = 256
NT = 32
KC = 4
NPTS = 16384
N_COL = 8


def draw_band_start(key, part):
    rows = jnp.arange(NT, dtype=jnp.int32)
    reach = jax.random.randint(key, (NT,), 1, NT // 2 + 1).astype(jnp.int32)
    reach = reach.at[NT // 2 + 1].set(NT)
    reach = reach.at[NT - 1].set(1)
    return jnp.maximum(rows - reach, 0).astype(jnp.int32)


def levels(rng, shape, pieces, low, largest):
    gain = 1.0
    for axis_at, parts in pieces:
        draws = jax.random.uniform(jax.random.fold_in(jax.random.fold_in(rng, 6), axis_at), (parts,), jnp.float32, low / len(pieces), largest / len(pieces))
        gain = gain * jnp.repeat(jnp.exp(draws), shape[axis_at] // parts).reshape((-1,) + (1,) * (len(shape) - 1 - axis_at))
    return gain


def bell_draw(rng, dims, deviation, most, shards=(), kind=jnp.bfloat16):
    array = deviation * jax.random.normal(rng, dims, jnp.float32)
    if shards:
        array = array * levels(rng, dims, shards, -0.22, 0.18)
    return jnp.clip(array, -most, most).astype(kind)


def setup_inputs(seed: int = 0) -> dict:
    seeds = jax.random.split(jax.random.key(seed), 5)
    points = bell_draw(seeds[0], (NPTS, COV), 1.0, 6.0, ((0, 32),), jnp.float32)
    nugget = jnp.clip(jnp.exp(math.log(2.0) - 1.3862944 * jax.random.uniform(seeds[1], (NPTS,), jnp.float32) ** levels(seeds[1], (NPTS,), ((0, 32),), -0.2, 0.2)), 0.5, 2.0)
    weights = jnp.clip(jnp.exp(jax.random.uniform(seeds[2], (COV,), jnp.float32, math.log(0.0005), math.log(0.005))), 0.0005, 0.005)
    band_start = draw_band_start(jax.random.fold_in(seeds[4], 71), 0)
    return {"points": points, "nugget": nugget, "weights": weights, "band_start": band_start}


def kernel_tile(xrow, xcol, weights):
    weighted = xrow * weights
    sq_row = lax.optimization_barrier(jnp.sum(weighted * xrow, axis=1))
    sq_col = lax.optimization_barrier(jnp.sum(xcol * xcol * weights, axis=1))
    cross = jnp.dot(weighted.astype(jnp.float32), xcol.T.astype(jnp.float32), precision=lax.Precision.HIGHEST, preferred_element_type=jnp.float32)
    dist_sq = jnp.maximum(sq_row[:, None] + sq_col[None, :] - 2.0 * cross, 0.0)
    dist = jnp.sqrt(3.0 * dist_sq)
    return (1.0 + dist) * jnp.exp(-dist)

def reference(points, nugget, weights, band_start):
    tiles_x = points.reshape(NT, TILE, COV)
    tiles_n = nugget.reshape(NT, TILE)
    indices = jnp.arange(NT, dtype=jnp.int32)

    def build_row(i):

        def build(j):
            block = kernel_tile(tiles_x[i], tiles_x[j], weights)
            keep = (j >= band_start[i]) & (j <= i)
            block = jnp.where(keep, block, jnp.float32(0.0))
            return block + jnp.where(j == i, jnp.diag(tiles_n[i]), jnp.float32(0.0))
        return lax.map(build, indices)
    matrix = lax.map(build_row, indices)
    for p in range(2):
        lpp = jnp.linalg.cholesky(matrix[p, p])
        solved = jax.vmap(lambda blk: jax.scipy.linalg.solve_triangular(lpp, blk.T, lower=True).T)(matrix[:, p])
        panel = jnp.where((indices > p)[:, None, None], solved, jnp.float32(0.0))
        panel = jnp.where((indices == p)[:, None, None], lpp[None], panel)

        def update(i):
            rowtiles = matrix[i]
            prod = jnp.einsum('ab,jcb->jac', panel[i], panel, precision=lax.Precision.HIGHEST)
            live = (indices > p) & (indices <= i)
            rowtiles = rowtiles - jnp.where(live[:, None, None], prod, jnp.float32(0.0))
            return jnp.where((indices == p)[:, None, None], panel[i][None], rowtiles)
        matrix = lax.map(update, indices)
    return matrix.reshape(NT, KC, N_COL, TILE, TILE)
```

```python
import jax
import jax.numpy as jnp
from jax import lax
from jax.sharding import PartitionSpec as P

HI = lax.Precision.HIGHEST


def mm(a, b):
    return lax.dot_general(
        a, b, (((1,), (1,)), ((), ())), precision=HI, preferred_element_type=jnp.float32
    )


def kernel_tile(xrow, xcol, weights):
    weighted = xrow * weights
    sq_row = jnp.sum(weighted * xrow, axis=1)
    sq_col = jnp.sum(xcol * xcol * weights, axis=1)
    cross = mm(weighted, xcol)
    dist_sq = jnp.maximum(sq_row[:, None] + sq_col[None, :] - 2.0 * cross, 0.0)
    dist = jnp.sqrt(3.0 * dist_sq)
    return (1.0 + dist) * jnp.exp(-dist)


def chol_inv(a):
    low = jnp.linalg.cholesky(a)
    eye = jnp.eye(a.shape[0], dtype=a.dtype)
    inv = jax.scipy.linalg.solve_triangular(low, eye, lower=True)
    return low, inv


def body(points, nugget, weights, band_start):
    n_row = lax.axis_size("row")
    n_col = lax.axis_size("col")
    blocks = n_row // n_col
    tile = points.shape[0]
    piece = tile // n_row
    my_row = lax.axis_index("row")
    my_col = lax.axis_index("col")

    chunks = points.reshape(n_row, piece, points.shape[1])
    recv = lax.all_to_all(chunks, "row", 0, 0, tiled=True)
    mine = lax.dynamic_slice_in_dim(
        recv.reshape(blocks, n_col, piece, points.shape[1]), my_col, 1, axis=1
    )[:, 0]
    sel = jnp.concatenate([recv[:2], mine], axis=0)
    tiles_x = lax.all_gather(sel, "row", axis=1, tiled=True)
    nug = lax.all_gather(nugget, "row", tiled=True)
    x0, x1 = tiles_x[0], tiles_x[1]
    xcols = tiles_x[2:]
    n0, n1 = nug[:tile], nug[tile : 2 * tile]

    cols = my_col + n_col * jnp.arange(blocks, dtype=jnp.int32)
    rows = jnp.concatenate([my_row[None], cols])
    xr_all = jnp.concatenate([points[None], xcols], axis=0).reshape(-1, points.shape[1])
    nr = len(rows)
    eye = jnp.eye(tile, dtype=jnp.float32)

    x01 = jnp.concatenate([x0, x1], axis=0)
    k01 = kernel_tile(x01, x01, weights)
    a00 = k01[:tile, :tile] + eye * n0[None, :]
    a10 = k01[tile:, :tile]
    a11 = k01[tile:, tile:] + eye * n1[None, :]

    kr = kernel_tile(xr_all, x01, weights).reshape(nr, tile, 2, tile)
    bs = band_start[rows]
    keep0 = (bs <= 0)[:, None, None]
    keep1 = ((bs <= 1) & (rows >= 1))[:, None, None]
    ar0 = jnp.where(keep0, kr[:, :, 0], 0.0)
    ar0 = ar0 + jnp.where((rows == 0)[:, None, None], eye * n0[None, :], 0.0)
    ar1 = jnp.where(keep1, kr[:, :, 1], 0.0)
    ar1 = ar1 + jnp.where((rows == 1)[:, None, None], eye * n1[None, :], 0.0)

    l00, m0 = chol_inv(a00)
    stack0 = jnp.concatenate([a10, ar0.reshape(-1, tile)], axis=0)
    sol0 = mm(stack0, m0)
    l01 = sol0[:tile]
    lr0 = sol0[tile:].reshape(nr, tile, tile)
    lr0 = jnp.where((rows == 0)[:, None, None], l00[None], lr0)

    s11 = a11 - mm(l01, l01)
    upd1 = mm(lr0.reshape(-1, tile), l01).reshape(nr, tile, tile)
    ar1 = ar1 - jnp.where((rows >= 1)[:, None, None], upd1, 0.0)
    l11, m1 = chol_inv(s11)
    lr1 = mm(ar1.reshape(-1, tile), m1).reshape(nr, tile, tile)
    lr1 = jnp.where((rows > 1)[:, None, None], lr1, jnp.where((rows == 1)[:, None, None], l11[None], 0.0))

    kout = kernel_tile(points, xcols.reshape(-1, points.shape[1]), weights)
    kout = kout.reshape(tile, blocks, tile).transpose(1, 0, 2)
    bsr = band_start[my_row]
    keep = ((cols >= bsr) & (cols <= my_row))[:, None, None]
    aout = jnp.where(keep, kout, 0.0)
    aout = aout + jnp.where((cols == my_row)[:, None, None], eye * nugget[None, :], 0.0)
    left = jnp.concatenate([lr0[0], lr1[0]], axis=1)
    right = jnp.concatenate([lr0[1:], lr1[1:]], axis=2).reshape(-1, 2 * tile)
    prod = mm(left, right).reshape(tile, blocks, tile).transpose(1, 0, 2)
    live = ((cols > 1) & (cols <= my_row))[:, None, None]
    res = aout - jnp.where(live, prod, 0.0)
    res = jnp.where((cols == 0)[:, None, None], lr0[0][None], res)
    res = jnp.where((cols == 1)[:, None, None], lr1[0][None], res)
    return res.reshape(1, blocks, 1, tile, tile)


def solution(mesh):
    placed = (P("row", None), P("row"), P(), P())
    return jax.shard_map(
        body,
        mesh=mesh,
        in_specs=placed,
        out_specs=P("row", None, "col", None, None),
        check_vma=False,
    )
```

```python
import jax
import jax.numpy as jnp
from jax import lax
from jax.sharding import PartitionSpec as P
from jax.experimental import pallas as pl
from jax.experimental.pallas import tpu as pltpu

HI = lax.Precision.HIGHEST


def mm(a, b):
    return lax.dot_general(
        a, b, (((1,), (1,)), ((), ())), precision=HI, preferred_element_type=jnp.float32
    )


def kernel_tile(xrow, xcol, weights):
    weighted = xrow * weights
    sq_row = jnp.sum(weighted * xrow, axis=1)
    sq_col = jnp.sum(xcol * xcol * weights, axis=1)
    cross = mm(weighted, xcol)
    dist_sq = jnp.maximum(sq_row[:, None] + sq_col[None, :] - 2.0 * cross, 0.0)
    dist = jnp.sqrt(3.0 * dist_sq)
    return (1.0 + dist) * jnp.exp(-dist)


BASE = 128
PHASE = 32


def _chol_base_kernel(a_ref, l_ref, m_ref, w_ref):
    n = a_ref.shape[0]
    w_ref[...] = a_ref[...]
    rows = lax.broadcasted_iota(jnp.int32, (n, n), 0)
    lanes = lax.broadcasted_iota(jnp.int32, (n, n), 1)
    m_ref[...] = jnp.where(rows == lanes, 1.0, 0.0).astype(jnp.float32)
    lane1 = lax.broadcasted_iota(jnp.int32, (1, n), 1)
    for q in range(n // PHASE):
        lo = q * PHASE
        size = n - lo
        sub_rows = lax.broadcasted_iota(jnp.int32, (size, 1), 0) + lo
        sub_lanes = lax.broadcasted_iota(jnp.int32, (size, n), 1)

        def step(j, carry, lo=lo, size=size, sub_rows=sub_rows, sub_lanes=sub_lanes):
            wrow = w_ref[pl.ds(j, 1), :]
            piv = jnp.sum(jnp.where(lane1 == j, wrow, 0.0), axis=1, keepdims=True)
            rs = lax.rsqrt(piv)
            lrow = jnp.where(lane1 >= j, wrow * rs, 0.0)
            w = w_ref[pl.ds(lo, size), :]
            wcol = jnp.sum(jnp.where(sub_lanes == j, w, 0.0), axis=1, keepdims=True)
            lcol = jnp.where(sub_rows > j, wcol * rs, 0.0)
            w_ref[pl.ds(lo, size), :] = w - lcol * lrow
            w_ref[pl.ds(j, 1), :] = lrow
            grow = m_ref[pl.ds(j, 1), :] * rs
            g = m_ref[pl.ds(lo, size), :]
            m_ref[pl.ds(lo, size), :] = g - lcol * grow
            m_ref[pl.ds(j, 1), :] = grow
            return carry

        lax.fori_loop(lo, lo + PHASE, step, 0)
    lt = jnp.where(lanes >= rows, w_ref[...], 0.0)
    l_ref[...] = lt.T
    m_ref[...] = jnp.where(rows >= lanes, m_ref[...], 0.0)


def chol_base(a):
    n = a.shape[0]
    return pl.pallas_call(
        _chol_base_kernel,
        out_shape=(
            jax.ShapeDtypeStruct((n, n), jnp.float32),
            jax.ShapeDtypeStruct((n, n), jnp.float32),
        ),
        scratch_shapes=[pltpu.VMEM((n, n), jnp.float32)],
    )(a)


def dot(a, b):
    return jnp.dot(a, b, precision=HI, preferred_element_type=jnp.float32)


def chol_inv(a):
    n = a.shape[0]
    if n <= BASE:
        return chol_base(a)
    h = n // 2
    l11, m11 = chol_inv(a[:h, :h])
    l21 = mm(a[h:, :h], m11)
    l22, m22 = chol_inv(a[h:, h:] - mm(l21, l21))
    m21 = -dot(dot(m22, l21), m11)
    zero = jnp.zeros((h, n - h), jnp.float32)
    low = jnp.concatenate([jnp.concatenate([l11, zero], 1), jnp.concatenate([l21, l22], 1)], 0)
    inv = jnp.concatenate([jnp.concatenate([m11, zero], 1), jnp.concatenate([m21, m22], 1)], 0)
    return low, inv


def body(points, nugget, weights, band_start):
    n_row = lax.axis_size("row")
    n_col = lax.axis_size("col")
    blocks = n_row // n_col
    tile = points.shape[0]
    piece = tile // n_row
    my_row = lax.axis_index("row")
    my_col = lax.axis_index("col")

    chunks = points.reshape(n_row, piece, points.shape[1])
    recv = lax.all_to_all(chunks, "row", 0, 0, tiled=True)
    mine = lax.dynamic_slice_in_dim(
        recv.reshape(blocks, n_col, piece, points.shape[1]), my_col, 1, axis=1
    )[:, 0]
    sel = jnp.concatenate([recv[:2], mine], axis=0)
    tiles_x = lax.all_gather(sel, "row", axis=1, tiled=True)
    nug = lax.all_gather(nugget, "row", tiled=True)
    x0, x1 = tiles_x[0], tiles_x[1]
    xcols = tiles_x[2:]
    n0, n1 = nug[:tile], nug[tile : 2 * tile]

    cols = my_col + n_col * jnp.arange(blocks, dtype=jnp.int32)
    rows = jnp.concatenate([my_row[None], cols])
    xr_all = jnp.concatenate([points[None], xcols], axis=0).reshape(-1, points.shape[1])
    nr = len(rows)
    eye = jnp.eye(tile, dtype=jnp.float32)

    x01 = jnp.concatenate([x0, x1], axis=0)
    k01 = kernel_tile(x01, x01, weights)
    a00 = k01[:tile, :tile] + eye * n0[None, :]
    a10 = k01[tile:, :tile]
    a11 = k01[tile:, tile:] + eye * n1[None, :]

    kr = kernel_tile(xr_all, x01, weights).reshape(nr, tile, 2, tile)
    bs = band_start[rows]
    keep0 = (bs <= 0)[:, None, None]
    keep1 = ((bs <= 1) & (rows >= 1))[:, None, None]
    ar0 = jnp.where(keep0, kr[:, :, 0], 0.0)
    ar0 = ar0 + jnp.where((rows == 0)[:, None, None], eye * n0[None, :], 0.0)
    ar1 = jnp.where(keep1, kr[:, :, 1], 0.0)
    ar1 = ar1 + jnp.where((rows == 1)[:, None, None], eye * n1[None, :], 0.0)

    l00, m0 = chol_inv(a00)
    stack0 = jnp.concatenate([a10, ar0.reshape(-1, tile)], axis=0)
    sol0 = mm(stack0, m0)
    l01 = sol0[:tile]
    lr0 = sol0[tile:].reshape(nr, tile, tile)
    lr0 = jnp.where((rows == 0)[:, None, None], l00[None], lr0)

    s11 = a11 - mm(l01, l01)
    upd1 = mm(lr0.reshape(-1, tile), l01).reshape(nr, tile, tile)
    ar1 = ar1 - jnp.where((rows >= 1)[:, None, None], upd1, 0.0)
    l11, m1 = chol_inv(s11)
    lr1 = mm(ar1.reshape(-1, tile), m1).reshape(nr, tile, tile)
    lr1 = jnp.where((rows > 1)[:, None, None], lr1, jnp.where((rows == 1)[:, None, None], l11[None], 0.0))

    kout = kernel_tile(points, xcols.reshape(-1, points.shape[1]), weights)
    kout = kout.reshape(tile, blocks, tile).transpose(1, 0, 2)
    bsr = band_start[my_row]
    keep = ((cols >= bsr) & (cols <= my_row))[:, None, None]
    aout = jnp.where(keep, kout, 0.0)
    aout = aout + jnp.where((cols == my_row)[:, None, None], eye * nugget[None, :], 0.0)
    left = jnp.concatenate([lr0[0], lr1[0]], axis=1)
    right = jnp.concatenate([lr0[1:], lr1[1:]], axis=2).reshape(-1, 2 * tile)
    prod = mm(left, right).reshape(tile, blocks, tile).transpose(1, 0, 2)
    live = ((cols > 1) & (cols <= my_row))[:, None, None]
    res = aout - jnp.where(live, prod, 0.0)
    res = jnp.where((cols == 0)[:, None, None], lr0[0][None], res)
    res = jnp.where((cols == 1)[:, None, None], lr1[0][None], res)
    return res.reshape(1, blocks, 1, tile, tile)


def solution(mesh):
    placed = (P("row", None), P("row"), P(), P())
    return jax.shard_map(
        body,
        mesh=mesh,
        in_specs=placed,
        out_specs=P("row", None, "col", None, None),
        check_vma=False,
    )
```

```python
import jax
import jax.numpy as jnp
from jax import lax
from jax.sharding import PartitionSpec as P
from jax.experimental import pallas as pl
from jax.experimental.pallas import tpu as pltpu

HI = lax.Precision.HIGHEST


def mm(a, b, precision=HI):
    return lax.dot_general(
        a, b, (((1,), (1,)), ((), ())), precision=precision, preferred_element_type=jnp.float32
    )


def kernel_tile(xrow, xcol, weights):
    weighted = xrow * weights
    sq_row = jnp.sum(weighted * xrow, axis=1)
    sq_col = jnp.sum(xcol * xcol * weights, axis=1)
    cross = mm(weighted, xcol, lax.Precision.HIGH)
    dist_sq = jnp.maximum(sq_row[:, None] + sq_col[None, :] - 2.0 * cross, 0.0)
    dist = jnp.sqrt(3.0 * dist_sq)
    return (1.0 + dist) * jnp.exp(-dist)


BASE = 128
PHASE = 32


def _chol_base_kernel(a_ref, l_ref, m_ref, w_ref):
    n = a_ref.shape[0]
    w_ref[...] = a_ref[...]
    rows = lax.broadcasted_iota(jnp.int32, (n, n), 0)
    lanes = lax.broadcasted_iota(jnp.int32, (n, n), 1)
    m_ref[...] = jnp.where(rows == lanes, 1.0, 0.0).astype(jnp.float32)
    lane1 = lax.broadcasted_iota(jnp.int32, (1, n), 1)
    for q in range(n // PHASE):
        lo = q * PHASE
        size = n - lo
        sub_rows = lax.broadcasted_iota(jnp.int32, (size, 1), 0) + lo
        sub_lanes = lax.broadcasted_iota(jnp.int32, (size, n), 1)

        def step(j, carry, lo=lo, size=size, sub_rows=sub_rows, sub_lanes=sub_lanes):
            wrow = w_ref[pl.ds(j, 1), :]
            piv = jnp.sum(jnp.where(lane1 == j, wrow, 0.0), axis=1, keepdims=True)
            rs = lax.rsqrt(piv)
            lrow = jnp.where(lane1 >= j, wrow * rs, 0.0)
            w = w_ref[pl.ds(lo, size), :]
            wcol = jnp.sum(jnp.where(sub_lanes == j, w, 0.0), axis=1, keepdims=True)
            lcol = jnp.where(sub_rows > j, wcol * rs, 0.0)
            w_ref[pl.ds(lo, size), :] = w - lcol * lrow
            w_ref[pl.ds(j, 1), :] = lrow
            grow = m_ref[pl.ds(j, 1), :] * rs
            g = m_ref[pl.ds(lo, size), :]
            m_ref[pl.ds(lo, size), :] = g - lcol * grow
            m_ref[pl.ds(j, 1), :] = grow
            return carry

        lax.fori_loop(lo, lo + PHASE, step, 0)
    lt = jnp.where(lanes >= rows, w_ref[...], 0.0)
    l_ref[...] = lt.T
    m_ref[...] = jnp.where(rows >= lanes, m_ref[...], 0.0)


def chol_base(a):
    n = a.shape[0]
    return pl.pallas_call(
        _chol_base_kernel,
        out_shape=(
            jax.ShapeDtypeStruct((n, n), jnp.float32),
            jax.ShapeDtypeStruct((n, n), jnp.float32),
        ),
        scratch_shapes=[pltpu.VMEM((n, n), jnp.float32)],
    )(a)


def dot(a, b):
    return jnp.dot(a, b, precision=HI, preferred_element_type=jnp.float32)


def chol_inv(a):
    n = a.shape[0]
    if n <= BASE:
        return chol_base(a)
    h = n // 2
    l11, m11 = chol_inv(a[:h, :h])
    l21 = mm(a[h:, :h], m11)
    l22, m22 = chol_inv(a[h:, h:] - mm(l21, l21))
    m21 = -dot(dot(m22, l21), m11)
    zero = jnp.zeros((h, n - h), jnp.float32)
    low = jnp.concatenate([jnp.concatenate([l11, zero], 1), jnp.concatenate([l21, l22], 1)], 0)
    inv = jnp.concatenate([jnp.concatenate([m11, zero], 1), jnp.concatenate([m21, m22], 1)], 0)
    return low, inv


def body(points, nugget, weights, band_start):
    n_row = lax.axis_size("row")
    n_col = lax.axis_size("col")
    blocks = n_row // n_col
    tile = points.shape[0]
    piece = tile // n_row
    my_row = lax.axis_index("row")
    my_col = lax.axis_index("col")

    chunks = points.reshape(n_row, piece, points.shape[1])
    recv = lax.all_to_all(chunks, "row", 0, 0, tiled=True)
    mine = lax.dynamic_slice_in_dim(
        recv.reshape(blocks, n_col, piece, points.shape[1]), my_col, 1, axis=1
    )[:, 0]
    sel = jnp.concatenate([recv[:2], mine], axis=0)
    tiles_x = lax.all_gather(sel, "row", axis=1, tiled=True)
    slot = jnp.arange(2, dtype=jnp.int32)[:, None] == my_row
    nug = lax.psum(jnp.where(slot, nugget[None, :], 0.0), "row")
    x0, x1 = tiles_x[0], tiles_x[1]
    xcols = tiles_x[2:]
    n0, n1 = nug[0], nug[1]

    cols = my_col + n_col * jnp.arange(blocks, dtype=jnp.int32)
    rows = jnp.concatenate([my_row[None], cols])
    xr_all = jnp.concatenate([points[None], xcols], axis=0).reshape(-1, points.shape[1])
    nr = len(rows)
    eye = jnp.eye(tile, dtype=jnp.float32)

    x01 = jnp.concatenate([x0, x1], axis=0)
    k01 = kernel_tile(x01, x01, weights)
    a00 = k01[:tile, :tile] + eye * n0[None, :]
    a10 = k01[tile:, :tile]
    a11 = k01[tile:, tile:] + eye * n1[None, :]

    kr = kernel_tile(xr_all, x01, weights).reshape(nr, tile, 2 * tile)
    bs = band_start[rows]
    keep0 = (bs <= 0)[:, None, None]
    keep1 = ((bs <= 1) & (rows >= 1))[:, None, None]
    ar0 = jnp.where(keep0, kr[:, :, :tile], 0.0)
    ar0 = ar0 + jnp.where((rows == 0)[:, None, None], eye * n0[None, :], 0.0)
    ar1 = jnp.where(keep1, kr[:, :, tile:], 0.0)
    ar1 = ar1 + jnp.where((rows == 1)[:, None, None], eye * n1[None, :], 0.0)

    l00, m0 = chol_inv(a00)
    stack0 = jnp.concatenate([a10, ar0.reshape(-1, tile)], axis=0)
    sol0 = mm(stack0, m0)
    l01 = sol0[:tile]
    lr0 = sol0[tile:].reshape(nr, tile, tile)
    lr0 = jnp.where((rows == 0)[:, None, None], l00[None], lr0)

    s11 = a11 - mm(l01, l01)
    upd1 = mm(lr0.reshape(-1, tile), l01).reshape(nr, tile, tile)
    ar1 = ar1 - jnp.where((rows >= 1)[:, None, None], upd1, 0.0)
    l11, m1 = chol_inv(s11)
    lr1 = mm(ar1.reshape(-1, tile), m1).reshape(nr, tile, tile)
    lr1 = jnp.where((rows > 1)[:, None, None], lr1, jnp.where((rows == 1)[:, None, None], l11[None], 0.0))

    kout = kernel_tile(points, xcols.reshape(-1, points.shape[1]), weights)
    kout = kout.reshape(tile, blocks, tile).transpose(1, 0, 2)
    bsr = band_start[my_row]
    keep = ((cols >= bsr) & (cols <= my_row))[:, None, None]
    aout = jnp.where(keep, kout, 0.0)
    aout = aout + jnp.where((cols == my_row)[:, None, None], eye * nugget[None, :], 0.0)
    left = jnp.concatenate([lr0[0], lr1[0]], axis=1)
    right = jnp.concatenate([lr0[1:], lr1[1:]], axis=2).reshape(-1, 2 * tile)
    prod = mm(left, right, lax.Precision.HIGH).reshape(tile, blocks, tile).transpose(1, 0, 2)
    live = ((cols > 1) & (cols <= my_row))[:, None, None]
    res = aout - jnp.where(live, prod, 0.0)
    res = jnp.where((cols == 0)[:, None, None], lr0[0][None], res)
    res = jnp.where((cols == 1)[:, None, None], lr1[0][None], res)
    return res.reshape(1, blocks, 1, tile, tile)


def solution(mesh):
    placed = (P("row", None), P("row"), P(), P())
    return jax.shard_map(
        body,
        mesh=mesh,
        in_specs=placed,
        out_specs=P("row", None, "col", None, None),
        check_vma=False,
    )
```

```python
import jax
import jax.numpy as jnp
from jax import lax
from jax.sharding import PartitionSpec as P
from jax.experimental import pallas as pl
from jax.experimental.pallas import tpu as pltpu

HI = lax.Precision.HIGHEST


def mm(a, b, precision=HI):
    return lax.dot_general(
        a, b, (((1,), (1,)), ((), ())), precision=precision, preferred_element_type=jnp.float32
    )


def kernel_tile(xrow, xcol, weights):
    weighted = xrow * weights
    sq_row = jnp.sum(weighted * xrow, axis=1)
    sq_col = jnp.sum(xcol * xcol * weights, axis=1)
    cross = mm(weighted, xcol, lax.Precision.HIGH)
    dist_sq = jnp.maximum(sq_row[:, None] + sq_col[None, :] - 2.0 * cross, 0.0)
    dist = jnp.sqrt(3.0 * dist_sq)
    return (1.0 + dist) * jnp.exp(-dist)


BASE = 128
PHASE = 32


def _chol_base_kernel(a_ref, l_ref, m_ref, w_ref):
    n = a_ref.shape[0]
    w_ref[...] = a_ref[...]
    rows = lax.broadcasted_iota(jnp.int32, (n, n), 0)
    lanes = lax.broadcasted_iota(jnp.int32, (n, n), 1)
    m_ref[...] = jnp.where(rows == lanes, 1.0, 0.0).astype(jnp.float32)
    lane1 = lax.broadcasted_iota(jnp.int32, (1, n), 1)
    for q in range(n // PHASE):
        lo = q * PHASE
        size = n - lo
        sub_rows = lax.broadcasted_iota(jnp.int32, (size, 1), 0) + lo
        sub_lanes = lax.broadcasted_iota(jnp.int32, (size, n), 1)

        def step(j, carry, lo=lo, size=size, sub_rows=sub_rows, sub_lanes=sub_lanes):
            wrow = w_ref[pl.ds(j, 1), :]
            piv = jnp.sum(jnp.where(lane1 == j, wrow, 0.0), axis=1, keepdims=True)
            rs = lax.rsqrt(piv)
            lrow = jnp.where(lane1 >= j, wrow * rs, 0.0)
            w = w_ref[pl.ds(lo, size), :]
            wcol = jnp.sum(jnp.where(sub_lanes == j, w, 0.0), axis=1, keepdims=True)
            lcol = jnp.where(sub_rows > j, wcol * rs, 0.0)
            w_ref[pl.ds(lo, size), :] = w - lcol * lrow
            w_ref[pl.ds(j, 1), :] = lrow
            grow = m_ref[pl.ds(j, 1), :] * rs
            g = m_ref[pl.ds(lo, size), :]
            m_ref[pl.ds(lo, size), :] = g - lcol * grow
            m_ref[pl.ds(j, 1), :] = grow
            return carry

        lax.fori_loop(lo, lo + PHASE, step, 0)
    lt = jnp.where(lanes >= rows, w_ref[...], 0.0)
    l_ref[...] = lt.T
    m_ref[...] = jnp.where(rows >= lanes, m_ref[...], 0.0)


def chol_base(a):
    n = a.shape[0]
    return pl.pallas_call(
        _chol_base_kernel,
        out_shape=(
            jax.ShapeDtypeStruct((n, n), jnp.float32),
            jax.ShapeDtypeStruct((n, n), jnp.float32),
        ),
        scratch_shapes=[pltpu.VMEM((n, n), jnp.float32)],
    )(a)


def dot(a, b):
    return jnp.dot(a, b, precision=HI, preferred_element_type=jnp.float32)


def chol_inv(a):
    n = a.shape[0]
    if n <= BASE:
        return chol_base(a)
    h = n // 2
    l11, m11 = chol_inv(a[:h, :h])
    l21 = mm(a[h:, :h], m11)
    l22, m22 = chol_inv(a[h:, h:] - mm(l21, l21))
    m21 = -dot(dot(m22, l21), m11)
    zero = jnp.zeros((h, n - h), jnp.float32)
    low = jnp.concatenate([jnp.concatenate([l11, zero], 1), jnp.concatenate([l21, l22], 1)], 0)
    inv = jnp.concatenate([jnp.concatenate([m11, zero], 1), jnp.concatenate([m21, m22], 1)], 0)
    return low, inv


def body(points, nugget, weights, band_start):
    n_row = lax.axis_size("row")
    n_col = lax.axis_size("col")
    blocks = n_row // n_col
    tile = points.shape[0]
    piece = tile // n_row
    my_row = lax.axis_index("row")
    my_col = lax.axis_index("col")

    slot = jnp.arange(2, dtype=jnp.int32)[:, None] == my_row
    nug = lax.psum(jnp.where(slot, nugget[None, :], 0.0), "row")
    n0, n1 = nug[0], nug[1]

    chunks = points.reshape(n_row, piece, points.shape[1])
    recv = lax.all_to_all(chunks, "row", 0, 0, tiled=True)
    tiles01 = lax.all_gather(recv[:2], "row", axis=1, tiled=True)
    mine = lax.dynamic_slice_in_dim(
        recv.reshape(blocks, n_col, piece, points.shape[1]), my_col, 1, axis=1
    )[:, 0]
    xcols = lax.all_gather(mine, "row", axis=1, tiled=True)
    x0, x1 = tiles01[0], tiles01[1]

    cols = my_col + n_col * jnp.arange(blocks, dtype=jnp.int32)
    rows = jnp.concatenate([my_row[None], cols])
    xr_all = jnp.concatenate([points[None], xcols], axis=0).reshape(-1, points.shape[1])
    nr = len(rows)
    eye = jnp.eye(tile, dtype=jnp.float32)

    x01 = jnp.concatenate([x0, x1], axis=0)
    k01 = kernel_tile(x01, x01, weights)
    a00 = k01[:tile, :tile] + eye * n0[None, :]
    a10 = k01[tile:, :tile]
    a11 = k01[tile:, tile:] + eye * n1[None, :]

    kr = kernel_tile(xr_all, x01, weights).reshape(nr, tile, 2 * tile)
    bs = band_start[rows]
    keep0 = (bs <= 0)[:, None, None]
    keep1 = ((bs <= 1) & (rows >= 1))[:, None, None]
    ar0 = jnp.where(keep0, kr[:, :, :tile], 0.0)
    ar0 = ar0 + jnp.where((rows == 0)[:, None, None], eye * n0[None, :], 0.0)
    ar1 = jnp.where(keep1, kr[:, :, tile:], 0.0)
    ar1 = ar1 + jnp.where((rows == 1)[:, None, None], eye * n1[None, :], 0.0)

    l00, m0 = chol_inv(a00)
    stack0 = jnp.concatenate([a10, ar0.reshape(-1, tile)], axis=0)
    sol0 = mm(stack0, m0)
    l01 = sol0[:tile]
    lr0 = sol0[tile:].reshape(nr, tile, tile)
    lr0 = jnp.where((rows == 0)[:, None, None], l00[None], lr0)

    s11 = a11 - mm(l01, l01)
    upd1 = mm(lr0.reshape(-1, tile), l01).reshape(nr, tile, tile)
    ar1 = ar1 - jnp.where((rows >= 1)[:, None, None], upd1, 0.0)
    l11, m1 = chol_inv(s11)
    lr1 = mm(ar1.reshape(-1, tile), m1).reshape(nr, tile, tile)
    lr1 = jnp.where((rows > 1)[:, None, None], lr1, jnp.where((rows == 1)[:, None, None], l11[None], 0.0))

    kout = kernel_tile(points, xcols.reshape(-1, points.shape[1]), weights)
    kout = kout.reshape(tile, blocks, tile).transpose(1, 0, 2)
    bsr = band_start[my_row]
    keep = ((cols >= bsr) & (cols <= my_row))[:, None, None]
    aout = jnp.where(keep, kout, 0.0)
    aout = aout + jnp.where((cols == my_row)[:, None, None], eye * nugget[None, :], 0.0)
    left = jnp.concatenate([lr0[0], lr1[0]], axis=1)
    right = jnp.concatenate([lr0[1:], lr1[1:]], axis=2).reshape(-1, 2 * tile)
    prod = mm(left, right, lax.Precision.HIGH).reshape(tile, blocks, tile).transpose(1, 0, 2)
    live = ((cols > 1) & (cols <= my_row))[:, None, None]
    res = aout - jnp.where(live, prod, 0.0)
    res = jnp.where((cols == 0)[:, None, None], lr0[0][None], res)
    res = jnp.where((cols == 1)[:, None, None], lr1[0][None], res)
    return res.reshape(1, blocks, 1, tile, tile)


def solution(mesh):
    placed = (P("row", None), P("row"), P(), P())
    return jax.shard_map(
        body,
        mesh=mesh,
        in_specs=placed,
        out_specs=P("row", None, "col", None, None),
        check_vma=False,
    )
```

```python
import jax
import jax.numpy as jnp
from jax import lax
from jax.sharding import PartitionSpec as P
from jax.experimental import pallas as pl
from jax.experimental.pallas import tpu as pltpu

HI = lax.Precision.HIGHEST


def mm(a, b, precision=HI):
    return lax.dot_general(
        a, b, (((1,), (1,)), ((), ())), precision=precision, preferred_element_type=jnp.float32
    )


def kernel_tile(xrow, xcol, weights):
    weighted = xrow * weights
    sq_row = jnp.sum(weighted * xrow, axis=1)
    sq_col = jnp.sum(xcol * xcol * weights, axis=1)
    cross = mm(weighted, xcol, lax.Precision.HIGH)
    dist_sq = jnp.maximum(sq_row[:, None] + sq_col[None, :] - 2.0 * cross, 0.0)
    dist = jnp.sqrt(3.0 * dist_sq)
    return (1.0 + dist) * jnp.exp(-dist)


BASE = 128
PHASE = 16


def _chol_base_kernel(a_ref, l_ref, m_ref, w_ref):
    n = a_ref.shape[0]
    w_ref[...] = a_ref[...]
    rows = lax.broadcasted_iota(jnp.int32, (n, n), 0)
    lanes = lax.broadcasted_iota(jnp.int32, (n, n), 1)
    m_ref[...] = jnp.where(rows == lanes, 1.0, 0.0).astype(jnp.float32)
    lane1 = lax.broadcasted_iota(jnp.int32, (1, n), 1)
    for q in range(n // PHASE):
        lo = q * PHASE
        size = n - lo
        sub_rows = lax.broadcasted_iota(jnp.int32, (size, 1), 0) + lo
        sub_lanes = lax.broadcasted_iota(jnp.int32, (size, n), 1)

        def step(j, carry, lo=lo, size=size, sub_rows=sub_rows, sub_lanes=sub_lanes):
            wrow = w_ref[pl.ds(j, 1), :]
            piv = jnp.sum(jnp.where(lane1 == j, wrow, 0.0), axis=1, keepdims=True)
            rs = lax.rsqrt(piv)
            lrow = jnp.where(lane1 >= j, wrow * rs, 0.0)
            w = w_ref[pl.ds(lo, size), :]
            wcol = jnp.sum(jnp.where(sub_lanes == j, w, 0.0), axis=1, keepdims=True)
            lcol = jnp.where(sub_rows > j, wcol * rs, 0.0)
            w_ref[pl.ds(lo, size), :] = w - lcol * lrow
            w_ref[pl.ds(j, 1), :] = lrow
            grow = m_ref[pl.ds(j, 1), :] * rs
            g = m_ref[pl.ds(lo, size), :]
            m_ref[pl.ds(lo, size), :] = g - lcol * grow
            m_ref[pl.ds(j, 1), :] = grow
            return carry

        lax.fori_loop(lo, lo + PHASE, step, 0)
    lt = jnp.where(lanes >= rows, w_ref[...], 0.0)
    l_ref[...] = lt.T
    m_ref[...] = jnp.where(rows >= lanes, m_ref[...], 0.0)


def chol_base(a):
    n = a.shape[0]
    return pl.pallas_call(
        _chol_base_kernel,
        out_shape=(
            jax.ShapeDtypeStruct((n, n), jnp.float32),
            jax.ShapeDtypeStruct((n, n), jnp.float32),
        ),
        scratch_shapes=[pltpu.VMEM((n, n), jnp.float32)],
    )(a)


def dot(a, b):
    return jnp.dot(a, b, precision=HI, preferred_element_type=jnp.float32)


def chol_inv(a):
    n = a.shape[0]
    if n <= BASE:
        return chol_base(a)
    h = n // 2
    l11, m11 = chol_inv(a[:h, :h])
    l21 = mm(a[h:, :h], m11)
    l22, m22 = chol_inv(a[h:, h:] - mm(l21, l21))
    m21 = -dot(dot(m22, l21), m11)
    zero = jnp.zeros((h, n - h), jnp.float32)
    low = jnp.concatenate([jnp.concatenate([l11, zero], 1), jnp.concatenate([l21, l22], 1)], 0)
    inv = jnp.concatenate([jnp.concatenate([m11, zero], 1), jnp.concatenate([m21, m22], 1)], 0)
    return low, inv


def body(points, nugget, weights, band_start):
    n_row = lax.axis_size("row")
    n_col = lax.axis_size("col")
    blocks = n_row // n_col
    tile = points.shape[0]
    piece = tile // n_row
    my_row = lax.axis_index("row")
    my_col = lax.axis_index("col")

    slot = jnp.arange(2, dtype=jnp.int32)[:, None] == my_row
    nug = lax.psum(jnp.where(slot, nugget[None, :], 0.0), "row")
    n0, n1 = nug[0], nug[1]

    chunks = points.reshape(n_row, piece, points.shape[1])
    recv = lax.all_to_all(chunks, "row", 0, 0, tiled=True)
    tiles01 = lax.all_gather(recv[:2] + 0.0 * nug[0, 0], "row", axis=1, tiled=True)
    mine = lax.dynamic_slice_in_dim(
        recv.reshape(blocks, n_col, piece, points.shape[1]), my_col, 1, axis=1
    )[:, 0]
    xcols = lax.all_gather(mine, "row", axis=1, tiled=True)
    x0, x1 = tiles01[0], tiles01[1]

    cols = my_col + n_col * jnp.arange(blocks, dtype=jnp.int32)
    rows = jnp.concatenate([my_row[None], cols])
    xr_all = jnp.concatenate([points[None], xcols], axis=0).reshape(-1, points.shape[1])
    nr = len(rows)
    eye = jnp.eye(tile, dtype=jnp.float32)

    x01 = jnp.concatenate([x0, x1], axis=0)
    k01 = kernel_tile(x01, x01, weights)
    a00 = k01[:tile, :tile] + eye * n0[None, :]
    a10 = k01[tile:, :tile]
    a11 = k01[tile:, tile:] + eye * n1[None, :]

    kr = kernel_tile(xr_all, x01, weights).reshape(nr, tile, 2 * tile)
    bs = band_start[rows]
    keep0 = (bs <= 0)[:, None, None]
    keep1 = ((bs <= 1) & (rows >= 1))[:, None, None]
    ar0 = jnp.where(keep0, kr[:, :, :tile], 0.0)
    ar0 = ar0 + jnp.where((rows == 0)[:, None, None], eye * n0[None, :], 0.0)
    ar1 = jnp.where(keep1, kr[:, :, tile:], 0.0)
    ar1 = ar1 + jnp.where((rows == 1)[:, None, None], eye * n1[None, :], 0.0)

    l00, m0 = chol_inv(a00)
    stack0 = jnp.concatenate([a10, ar0.reshape(-1, tile)], axis=0)
    sol0 = mm(stack0, m0)
    l01 = sol0[:tile]
    lr0 = sol0[tile:].reshape(nr, tile, tile)
    lr0 = jnp.where((rows == 0)[:, None, None], l00[None], lr0)

    s11 = a11 - mm(l01, l01)
    upd1 = mm(lr0.reshape(-1, tile), l01).reshape(nr, tile, tile)
    ar1 = ar1 - jnp.where((rows >= 1)[:, None, None], upd1, 0.0)
    l11, m1 = chol_inv(s11)
    lr1 = mm(ar1.reshape(-1, tile), m1).reshape(nr, tile, tile)
    lr1 = jnp.where((rows > 1)[:, None, None], lr1, jnp.where((rows == 1)[:, None, None], l11[None], 0.0))

    kout = kernel_tile(points, xcols.reshape(-1, points.shape[1]), weights)
    kout = kout.reshape(tile, blocks, tile).transpose(1, 0, 2)
    bsr = band_start[my_row]
    keep = ((cols >= bsr) & (cols <= my_row))[:, None, None]
    aout = jnp.where(keep, kout, 0.0)
    aout = aout + jnp.where((cols == my_row)[:, None, None], eye * nugget[None, :], 0.0)
    left = jnp.concatenate([lr0[0], lr1[0]], axis=1)
    right = jnp.concatenate([lr0[1:], lr1[1:]], axis=2).reshape(-1, 2 * tile)
    prod = mm(left, right, lax.Precision.HIGH).reshape(tile, blocks, tile).transpose(1, 0, 2)
    live = ((cols > 1) & (cols <= my_row))[:, None, None]
    res = aout - jnp.where(live, prod, 0.0)
    res = jnp.where((cols == 0)[:, None, None], lr0[0][None], res)
    res = jnp.where((cols == 1)[:, None, None], lr1[0][None], res)
    return res.reshape(1, blocks, 1, tile, tile)


def solution(mesh):
    placed = (P("row", None), P("row"), P(), P())
    return jax.shard_map(
        body,
        mesh=mesh,
        in_specs=placed,
        out_specs=P("row", None, "col", None, None),
        check_vma=False,
    )
```

```python
import jax
import jax.numpy as jnp
from jax import lax
from jax.sharding import PartitionSpec as P
from jax.experimental import pallas as pl
from jax.experimental.pallas import tpu as pltpu

HI = lax.Precision.HIGHEST


def mm(a, b, precision=HI):
    return lax.dot_general(
        a, b, (((1,), (1,)), ((), ())), precision=precision, preferred_element_type=jnp.float32
    )


def kernel_tile(xrow, xcol, weights):
    weighted = xrow * weights
    sq_row = jnp.sum(weighted * xrow, axis=1)
    sq_col = jnp.sum(xcol * xcol * weights, axis=1)
    cross = mm(weighted, xcol, lax.Precision.HIGH)
    dist_sq = jnp.maximum(sq_row[:, None] + sq_col[None, :] - 2.0 * cross, 0.0)
    dist = jnp.sqrt(3.0 * dist_sq)
    return (1.0 + dist) * jnp.exp(-dist)


BASE = 128
PHASE = 32


def _chol_base_kernel(a_ref, l_ref, m_ref, w_ref):
    n = a_ref.shape[0]
    w_ref[...] = a_ref[...]
    rows = lax.broadcasted_iota(jnp.int32, (n, n), 0)
    lanes = lax.broadcasted_iota(jnp.int32, (n, n), 1)
    m_ref[...] = jnp.where(rows == lanes, 1.0, 0.0).astype(jnp.float32)
    lane1 = lax.broadcasted_iota(jnp.int32, (1, n), 1)
    for q in range(n // PHASE):
        lo = q * PHASE
        size = n - lo
        sub_rows = lax.broadcasted_iota(jnp.int32, (size, 1), 0) + lo
        sub_lanes = lax.broadcasted_iota(jnp.int32, (size, n), 1)

        def step(j, carry, lo=lo, size=size, sub_rows=sub_rows, sub_lanes=sub_lanes):
            wrow = w_ref[pl.ds(j, 1), :]
            piv = jnp.sum(jnp.where(lane1 == j, wrow, 0.0), axis=1, keepdims=True)
            rs = lax.rsqrt(piv)
            lrow = jnp.where(lane1 >= j, wrow * rs, 0.0)
            w = w_ref[pl.ds(lo, size), :]
            wcol = jnp.sum(jnp.where(sub_lanes == j, w, 0.0), axis=1, keepdims=True)
            lcol = jnp.where(sub_rows > j, wcol * rs, 0.0)
            w_ref[pl.ds(lo, size), :] = w - lcol * lrow
            w_ref[pl.ds(j, 1), :] = lrow
            grow = m_ref[pl.ds(j, 1), :] * rs
            g = m_ref[pl.ds(lo, size), :]
            m_ref[pl.ds(lo, size), :] = g - lcol * grow
            m_ref[pl.ds(j, 1), :] = grow
            return carry

        lax.fori_loop(lo, lo + PHASE, step, 0)
    lt = jnp.where(lanes >= rows, w_ref[...], 0.0)
    l_ref[...] = lt.T
    m_ref[...] = jnp.where(rows >= lanes, m_ref[...], 0.0)


def chol_base(a):
    n = a.shape[0]
    return pl.pallas_call(
        _chol_base_kernel,
        out_shape=(
            jax.ShapeDtypeStruct((n, n), jnp.float32),
            jax.ShapeDtypeStruct((n, n), jnp.float32),
        ),
        scratch_shapes=[pltpu.VMEM((n, n), jnp.float32)],
    )(a)


def dot(a, b):
    return jnp.dot(a, b, precision=HI, preferred_element_type=jnp.float32)


def chol_inv(a):
    n = a.shape[0]
    if n <= BASE:
        return chol_base(a)
    h = n // 2
    l11, m11 = chol_inv(a[:h, :h])
    l21 = mm(a[h:, :h], m11)
    l22, m22 = chol_inv(a[h:, h:] - mm(l21, l21))
    m21 = -dot(dot(m22, l21), m11)
    zero = jnp.zeros((h, n - h), jnp.float32)
    low = jnp.concatenate([jnp.concatenate([l11, zero], 1), jnp.concatenate([l21, l22], 1)], 0)
    inv = jnp.concatenate([jnp.concatenate([m11, zero], 1), jnp.concatenate([m21, m22], 1)], 0)
    return low, inv


def body(points, nugget, weights, band_start):
    n_row = lax.axis_size("row")
    n_col = lax.axis_size("col")
    blocks = n_row // n_col
    tile, cov = points.shape
    piece = tile // n_row
    my_row = lax.axis_index("row")
    my_col = lax.axis_index("col")

    flat = points.reshape(n_row, piece * cov)
    nug_pad = jnp.pad(nugget.reshape(n_row, piece), ((0, 0), (0, 128 - piece)))
    recv = lax.all_to_all(jnp.concatenate([flat, nug_pad], axis=1), "row", 0, 0, tiled=True)
    width = recv.shape[1]
    mine = lax.dynamic_slice_in_dim(recv.reshape(blocks, n_col, width), my_col, 1, axis=1)[:, 0]
    sel = jnp.concatenate([recv[:2], mine], axis=0)
    got = lax.all_gather(sel, "row", axis=1)
    xs = got[:, :, : piece * cov].reshape(2 + blocks, tile, cov)
    ns = got[:, :, piece * cov : piece * cov + piece].reshape(2 + blocks, tile)
    x0, x1 = xs[0], xs[1]
    xcols = xs[2:]
    n0, n1 = ns[0], ns[1]

    cols = my_col + n_col * jnp.arange(blocks, dtype=jnp.int32)
    rows = jnp.concatenate([my_row[None], cols])
    nr = len(rows)
    xr_all = jnp.concatenate([points[None], xcols], axis=0).reshape(nr * tile, cov)
    eye = jnp.eye(tile, dtype=jnp.float32)
    rmask = lambda m: m[:, None, None]

    a00 = kernel_tile(x0, x0, weights) + eye * n0[None, :]
    a10 = kernel_tile(x1, x0, weights)
    a11 = kernel_tile(x1, x1, weights) + eye * n1[None, :]

    bs = band_start[rows]
    kr0 = kernel_tile(xr_all, x0, weights).reshape(nr, tile, tile)
    ar0 = jnp.where(rmask(bs <= 0), kr0, 0.0) + jnp.where(rmask(rows == 0), eye * n0[None, :], 0.0)
    kr1 = kernel_tile(xr_all, x1, weights).reshape(nr, tile, tile)
    ar1 = jnp.where(rmask((bs <= 1) & (rows >= 1)), kr1, 0.0)
    ar1 = ar1 + jnp.where(rmask(rows == 1), eye * n1[None, :], 0.0)

    l00, m0 = chol_inv(a00)
    l01 = mm(a10, m0)
    lr0 = mm(ar0.reshape(nr * tile, tile), m0).reshape(nr, tile, tile)
    lr0 = jnp.where(rmask(rows == 0), l00[None], lr0)

    l11, m1 = chol_inv(a11 - mm(l01, l01))
    upd1 = mm(lr0.reshape(nr * tile, tile), l01).reshape(nr, tile, tile)
    ar1 = ar1 - jnp.where(rmask(rows >= 1), upd1, 0.0)
    lr1 = mm(ar1.reshape(nr * tile, tile), m1).reshape(nr, tile, tile)
    lr1 = jnp.where(rmask(rows > 1), lr1, jnp.where(rmask(rows == 1), l11[None], 0.0))

    bsr = band_start[my_row]
    out = []
    for k in range(blocks):
        col = cols[k]
        a = kernel_tile(points, xcols[k], weights)
        a = jnp.where((col >= bsr) & (col <= my_row), a, 0.0)
        a = a + jnp.where(col == my_row, eye * nugget[None, :], 0.0)
        prod = mm(lr0[0], lr0[1 + k], lax.Precision.HIGH) + mm(lr1[0], lr1[1 + k], lax.Precision.HIGH)
        res = a - jnp.where((col > 1) & (col <= my_row), prod, 0.0)
        res = jnp.where(col == 0, lr0[0], jnp.where(col == 1, lr1[0], res))
        out.append(res)
    return jnp.stack(out).reshape(1, blocks, 1, tile, tile)


def solution(mesh):
    placed = (P("row", None), P("row"), P(), P())
    return jax.shard_map(
        body,
        mesh=mesh,
        in_specs=placed,
        out_specs=P("row", None, "col", None, None),
        check_vma=False,
    )
```

```python
import jax
import jax.numpy as jnp
from jax import lax
from jax.sharding import PartitionSpec as P
from jax.experimental import pallas as pl
from jax.experimental.pallas import tpu as pltpu

HI = lax.Precision.HIGHEST


def mm(a, b, precision=HI):
    return lax.dot_general(
        a, b, (((1,), (1,)), ((), ())), precision=precision, preferred_element_type=jnp.float32
    )


def kernel_tile(xrow, xcol, weights):
    weighted = xrow * weights
    sq_row = jnp.sum(weighted * xrow, axis=1)
    sq_col = jnp.sum(xcol * xcol * weights, axis=1)
    cross = mm(weighted, xcol, lax.Precision.HIGH)
    dist_sq = jnp.maximum(sq_row[:, None] + sq_col[None, :] - 2.0 * cross, 0.0)
    dist = jnp.sqrt(3.0 * dist_sq)
    return (1.0 + dist) * jnp.exp(-dist)


BASE = 128
PHASE = 32
NPIV = 4


def _chol_base_kernel(a_ref, l_ref, m_ref, w_ref):
    n = a_ref.shape[0]
    w_ref[...] = a_ref[...]
    rows = lax.broadcasted_iota(jnp.int32, (n, n), 0)
    lanes = lax.broadcasted_iota(jnp.int32, (n, n), 1)
    m_ref[...] = jnp.where(rows == lanes, 1.0, 0.0).astype(jnp.float32)
    lane1 = lax.broadcasted_iota(jnp.int32, (1, n), 1)
    for q in range(n // PHASE):
        lo = q * PHASE
        size = n - lo
        sub_rows = lax.broadcasted_iota(jnp.int32, (size, 1), 0) + lo
        sub_lanes = lax.broadcasted_iota(jnp.int32, (size, n), 1)

        def step(i, carry, lo=lo, size=size, sub_rows=sub_rows, sub_lanes=sub_lanes):
            j = lo + NPIV * i
            r = [w_ref[pl.ds(j + t, 1), :] for t in range(NPIV)]
            blk = [
                [jnp.sum(jnp.where(lane1 == j + u, r[t], 0.0), axis=1, keepdims=True) for u in range(t + 1)]
                for t in range(NPIV)
            ]
            w = w_ref[pl.ds(lo, size), :]
            wc = [
                jnp.sum(jnp.where(sub_lanes == j + t, w, 0.0), axis=1, keepdims=True)
                for t in range(NPIV)
            ]
            low = [[None] * NPIV for _ in range(NPIV)]
            rs = [None] * NPIV
            for t in range(NPIV):
                for u in range(t):
                    acc = blk[t][u]
                    for v in range(u):
                        acc = acc - low[t][v] * low[u][v]
                    low[t][u] = acc * rs[u]
                acc = blk[t][t]
                for v in range(t):
                    acc = acc - low[t][v] * low[t][v]
                rs[t] = lax.rsqrt(acc)
            below = sub_rows > j + NPIV - 1
            urow, crow, grow = [], [], []
            for t in range(NPIV):
                ut, ct = r[t], wc[t]
                gt = m_ref[pl.ds(j + t, 1), :]
                for v in range(t):
                    ut = ut - low[t][v] * urow[v]
                    ct = ct - crow[v] * low[t][v]
                    gt = gt - low[t][v] * grow[v]
                urow.append(jnp.where(lane1 >= j + t, ut * rs[t], 0.0))
                crow.append(ct * rs[t])
                grow.append(gt * rs[t])
            crow = [jnp.where(below, ct, 0.0) for ct in crow]
            g = m_ref[pl.ds(lo, size), :]
            for t in range(NPIV):
                w = w - crow[t] * urow[t]
                g = g - crow[t] * grow[t]
            w_ref[pl.ds(lo, size), :] = w
            m_ref[pl.ds(lo, size), :] = g
            for t in range(NPIV):
                w_ref[pl.ds(j + t, 1), :] = urow[t]
                m_ref[pl.ds(j + t, 1), :] = grow[t]
            return carry

        lax.fori_loop(0, PHASE // NPIV, step, 0)
    lt = jnp.where(lanes >= rows, w_ref[...], 0.0)
    l_ref[...] = lt.T
    m_ref[...] = jnp.where(rows >= lanes, m_ref[...], 0.0)


def chol_base(a):
    n = a.shape[0]
    return pl.pallas_call(
        _chol_base_kernel,
        out_shape=(
            jax.ShapeDtypeStruct((n, n), jnp.float32),
            jax.ShapeDtypeStruct((n, n), jnp.float32),
        ),
        scratch_shapes=[pltpu.VMEM((n, n), jnp.float32)],
    )(a)


def dot(a, b):
    return jnp.dot(a, b, precision=HI, preferred_element_type=jnp.float32)


def chol_inv(a):
    n = a.shape[0]
    if n <= BASE:
        return chol_base(a)
    h = n // 2
    l11, m11 = chol_inv(a[:h, :h])
    l21 = mm(a[h:, :h], m11)
    l22, m22 = chol_inv(a[h:, h:] - mm(l21, l21))
    m21 = -dot(dot(m22, l21), m11)
    zero = jnp.zeros((h, n - h), jnp.float32)
    low = jnp.concatenate([jnp.concatenate([l11, zero], 1), jnp.concatenate([l21, l22], 1)], 0)
    inv = jnp.concatenate([jnp.concatenate([m11, zero], 1), jnp.concatenate([m21, m22], 1)], 0)
    return low, inv


def body(points, nugget, weights, band_start):
    n_row = lax.axis_size("row")
    n_col = lax.axis_size("col")
    blocks = n_row // n_col
    tile, cov = points.shape
    piece = tile // n_row
    my_row = lax.axis_index("row")
    my_col = lax.axis_index("col")

    flat = points.reshape(n_row, piece * cov)
    nug_pad = jnp.pad(nugget.reshape(n_row, piece), ((0, 0), (0, 128 - piece)))
    recv = lax.all_to_all(jnp.concatenate([flat, nug_pad], axis=1), "row", 0, 0, tiled=True)
    width = recv.shape[1]
    mine = lax.dynamic_slice_in_dim(recv.reshape(blocks, n_col, width), my_col, 1, axis=1)[:, 0]
    sel = jnp.concatenate([recv[:2], mine], axis=0)
    got = lax.all_gather(sel, "row", axis=1)
    xs = got[:, :, : piece * cov].reshape(2 + blocks, tile, cov)
    ns = got[:, :, piece * cov : piece * cov + piece].reshape(2 + blocks, tile)
    x0, x1 = xs[0], xs[1]
    xcols = xs[2:]
    n0, n1 = ns[0], ns[1]

    cols = my_col + n_col * jnp.arange(blocks, dtype=jnp.int32)
    rows = jnp.concatenate([my_row[None], cols])
    nr = len(rows)
    xr_all = jnp.concatenate([points[None], xcols], axis=0).reshape(nr * tile, cov)
    eye = jnp.eye(tile, dtype=jnp.float32)
    rmask = lambda m: m[:, None, None]

    a00 = kernel_tile(x0, x0, weights) + eye * n0[None, :]
    a10 = kernel_tile(x1, x0, weights)
    a11 = kernel_tile(x1, x1, weights) + eye * n1[None, :]

    bs = band_start[rows]
    kr0 = kernel_tile(xr_all, x0, weights).reshape(nr, tile, tile)
    ar0 = jnp.where(rmask(bs <= 0), kr0, 0.0) + jnp.where(rmask(rows == 0), eye * n0[None, :], 0.0)
    kr1 = kernel_tile(xr_all, x1, weights).reshape(nr, tile, tile)
    ar1 = jnp.where(rmask((bs <= 1) & (rows >= 1)), kr1, 0.0)
    ar1 = ar1 + jnp.where(rmask(rows == 1), eye * n1[None, :], 0.0)

    l00, m0 = chol_inv(a00)
    l01 = mm(a10, m0)
    lr0 = mm(ar0.reshape(nr * tile, tile), m0).reshape(nr, tile, tile)
    lr0 = jnp.where(rmask(rows == 0), l00[None], lr0)

    l11, m1 = chol_inv(a11 - mm(l01, l01))
    upd1 = mm(lr0.reshape(nr * tile, tile), l01, lax.Precision.HIGH).reshape(nr, tile, tile)
    ar1 = ar1 - jnp.where(rmask(rows >= 1), upd1, 0.0)
    lr1 = mm(ar1.reshape(nr * tile, tile), m1).reshape(nr, tile, tile)
    lr1 = jnp.where(rmask(rows > 1), lr1, jnp.where(rmask(rows == 1), l11[None], 0.0))

    bsr = band_start[my_row]
    out = []
    for k in range(blocks):
        col = cols[k]
        a = kernel_tile(points, xcols[k], weights)
        a = jnp.where((col >= bsr) & (col <= my_row), a, 0.0)
        a = a + jnp.where(col == my_row, eye * nugget[None, :], 0.0)
        prod = mm(lr0[0], lr0[1 + k], lax.Precision.HIGH) + mm(lr1[0], lr1[1 + k], lax.Precision.HIGH)
        res = a - jnp.where((col > 1) & (col <= my_row), prod, 0.0)
        res = jnp.where(col == 0, lr0[0], jnp.where(col == 1, lr1[0], res))
        out.append(res)
    return jnp.stack(out).reshape(1, blocks, 1, tile, tile)


def solution(mesh):
    placed = (P("row", None), P("row"), P(), P())
    return jax.shard_map(
        body,
        mesh=mesh,
        in_specs=placed,
        out_specs=P("row", None, "col", None, None),
        check_vma=False,
    )
```

```python
import jax
import jax.numpy as jnp
from jax import lax
from jax.sharding import PartitionSpec as P
from jax.experimental import pallas as pl
from jax.experimental.pallas import tpu as pltpu

HI = lax.Precision.HIGHEST


def mm(a, b, precision=HI):
    return lax.dot_general(
        a, b, (((1,), (1,)), ((), ())), precision=precision, preferred_element_type=jnp.float32
    )


def kernel_tile(xrow, xcol, weights):
    weighted = xrow * weights
    sq_row = jnp.sum(weighted * xrow, axis=1)
    sq_col = jnp.sum(xcol * xcol * weights, axis=1)
    cross = mm(weighted, xcol, lax.Precision.HIGH)
    dist_sq = jnp.maximum(sq_row[:, None] + sq_col[None, :] - 2.0 * cross, 0.0)
    dist = jnp.sqrt(3.0 * dist_sq)
    return (1.0 + dist) * jnp.exp(-dist)


BASE = 128
PHASE = 32
NPIV = 8


def _chol_base_kernel(a_ref, l_ref, m_ref, w_ref):
    n = a_ref.shape[0]
    w_ref[...] = a_ref[...]
    rows = lax.broadcasted_iota(jnp.int32, (n, n), 0)
    lanes = lax.broadcasted_iota(jnp.int32, (n, n), 1)
    m_ref[...] = jnp.where(rows == lanes, 1.0, 0.0).astype(jnp.float32)
    lane1 = lax.broadcasted_iota(jnp.int32, (1, n), 1)
    for q in range(n // PHASE):
        lo = q * PHASE
        size = n - lo
        sub_rows = lax.broadcasted_iota(jnp.int32, (size, 1), 0) + lo
        sub_lanes = lax.broadcasted_iota(jnp.int32, (size, n), 1)

        def step(i, carry, lo=lo, size=size, sub_rows=sub_rows, sub_lanes=sub_lanes):
            j = lo + NPIV * i
            r = [w_ref[pl.ds(j + t, 1), :] for t in range(NPIV)]
            blk = [
                [jnp.sum(jnp.where(lane1 == j + u, r[t], 0.0), axis=1, keepdims=True) for u in range(t + 1)]
                for t in range(NPIV)
            ]
            w = w_ref[pl.ds(lo, size), :]
            wc = [
                jnp.sum(jnp.where(sub_lanes == j + t, w, 0.0), axis=1, keepdims=True)
                for t in range(NPIV)
            ]
            low = [[None] * NPIV for _ in range(NPIV)]
            rs = [None] * NPIV
            for t in range(NPIV):
                for u in range(t):
                    acc = blk[t][u]
                    for v in range(u):
                        acc = acc - low[t][v] * low[u][v]
                    low[t][u] = acc * rs[u]
                acc = blk[t][t]
                for v in range(t):
                    acc = acc - low[t][v] * low[t][v]
                rs[t] = lax.rsqrt(acc)
            below = sub_rows > j + NPIV - 1
            urow, crow, grow = [], [], []
            for t in range(NPIV):
                ut, ct = r[t], wc[t]
                gt = m_ref[pl.ds(j + t, 1), :]
                for v in range(t):
                    ut = ut - low[t][v] * urow[v]
                    ct = ct - crow[v] * low[t][v]
                    gt = gt - low[t][v] * grow[v]
                urow.append(jnp.where(lane1 >= j + t, ut * rs[t], 0.0))
                crow.append(ct * rs[t])
                grow.append(gt * rs[t])
            crow = [jnp.where(below, ct, 0.0) for ct in crow]
            g = m_ref[pl.ds(lo, size), :]
            for t in range(NPIV):
                w = w - crow[t] * urow[t]
                g = g - crow[t] * grow[t]
            w_ref[pl.ds(lo, size), :] = w
            m_ref[pl.ds(lo, size), :] = g
            for t in range(NPIV):
                w_ref[pl.ds(j + t, 1), :] = urow[t]
                m_ref[pl.ds(j + t, 1), :] = grow[t]
            return carry

        lax.fori_loop(0, PHASE // NPIV, step, 0)
    lt = jnp.where(lanes >= rows, w_ref[...], 0.0)
    l_ref[...] = lt.T
    m_ref[...] = jnp.where(rows >= lanes, m_ref[...], 0.0)


def chol_base(a):
    n = a.shape[0]
    return pl.pallas_call(
        _chol_base_kernel,
        out_shape=(
            jax.ShapeDtypeStruct((n, n), jnp.float32),
            jax.ShapeDtypeStruct((n, n), jnp.float32),
        ),
        scratch_shapes=[pltpu.VMEM((n, n), jnp.float32)],
    )(a)


def dot(a, b):
    return jnp.dot(a, b, precision=HI, preferred_element_type=jnp.float32)


def chol_inv(a):
    n = a.shape[0]
    if n <= BASE:
        return chol_base(a)
    h = n // 2
    l11, m11 = chol_inv(a[:h, :h])
    l21 = mm(a[h:, :h], m11)
    l22, m22 = chol_inv(a[h:, h:] - mm(l21, l21))
    m21 = -dot(dot(m22, l21), m11)
    zero = jnp.zeros((h, n - h), jnp.float32)
    low = jnp.concatenate([jnp.concatenate([l11, zero], 1), jnp.concatenate([l21, l22], 1)], 0)
    inv = jnp.concatenate([jnp.concatenate([m11, zero], 1), jnp.concatenate([m21, m22], 1)], 0)
    return low, inv


def body(points, nugget, weights, band_start):
    n_row = lax.axis_size("row")
    n_col = lax.axis_size("col")
    blocks = n_row // n_col
    tile, cov = points.shape
    piece = tile // n_row
    my_row = lax.axis_index("row")
    my_col = lax.axis_index("col")

    flat = points.reshape(n_row, piece * cov)
    nug_pad = jnp.pad(nugget.reshape(n_row, piece), ((0, 0), (0, 128 - piece)))
    recv = lax.all_to_all(jnp.concatenate([flat, nug_pad], axis=1), "row", 0, 0, tiled=True)
    width = recv.shape[1]
    mine = lax.dynamic_slice_in_dim(recv.reshape(blocks, n_col, width), my_col, 1, axis=1)[:, 0]
    sel = jnp.concatenate([recv[:2], mine], axis=0)
    got = lax.all_gather(sel, "row", axis=1)
    xs = got[:, :, : piece * cov].reshape(2 + blocks, tile, cov)
    ns = got[:, :, piece * cov : piece * cov + piece].reshape(2 + blocks, tile)
    x0, x1 = xs[0], xs[1]
    xcols = xs[2:]
    n0, n1 = ns[0], ns[1]

    cols = my_col + n_col * jnp.arange(blocks, dtype=jnp.int32)
    rows = jnp.concatenate([my_row[None], cols])
    nr = len(rows)
    xr_all = jnp.concatenate([points[None], xcols], axis=0).reshape(nr * tile, cov)
    eye = jnp.eye(tile, dtype=jnp.float32)
    rmask = lambda m: m[:, None, None]

    a00 = kernel_tile(x0, x0, weights) + eye * n0[None, :]
    a10 = kernel_tile(x1, x0, weights)
    a11 = kernel_tile(x1, x1, weights) + eye * n1[None, :]

    bs = band_start[rows]
    kr0 = kernel_tile(xr_all, x0, weights).reshape(nr, tile, tile)
    ar0 = jnp.where(rmask(bs <= 0), kr0, 0.0) + jnp.where(rmask(rows == 0), eye * n0[None, :], 0.0)
    kr1 = kernel_tile(xr_all, x1, weights).reshape(nr, tile, tile)
    ar1 = jnp.where(rmask((bs <= 1) & (rows >= 1)), kr1, 0.0)
    ar1 = ar1 + jnp.where(rmask(rows == 1), eye * n1[None, :], 0.0)

    l00, m0 = chol_inv(a00)
    l01 = mm(a10, m0)
    lr0 = mm(ar0.reshape(nr * tile, tile), m0).reshape(nr, tile, tile)
    lr0 = jnp.where(rmask(rows == 0), l00[None], lr0)

    l11, m1 = chol_inv(a11 - mm(l01, l01))
    upd1 = mm(lr0.reshape(nr * tile, tile), l01, lax.Precision.HIGH).reshape(nr, tile, tile)
    ar1 = ar1 - jnp.where(rmask(rows >= 1), upd1, 0.0)
    lr1 = mm(ar1.reshape(nr * tile, tile), m1).reshape(nr, tile, tile)
    lr1 = jnp.where(rmask(rows > 1), lr1, jnp.where(rmask(rows == 1), l11[None], 0.0))

    bsr = band_start[my_row]
    out = []
    for k in range(blocks):
        col = cols[k]
        a = kernel_tile(points, xcols[k], weights)
        a = jnp.where((col >= bsr) & (col <= my_row), a, 0.0)
        a = a + jnp.where(col == my_row, eye * nugget[None, :], 0.0)
        prod = mm(lr0[0], lr0[1 + k], lax.Precision.HIGH) + mm(lr1[0], lr1[1 + k], lax.Precision.HIGH)
        res = a - jnp.where((col > 1) & (col <= my_row), prod, 0.0)
        res = jnp.where(col == 0, lr0[0], jnp.where(col == 1, lr1[0], res))
        out.append(res)
    return jnp.stack(out).reshape(1, blocks, 1, tile, tile)


def solution(mesh):
    placed = (P("row", None), P("row"), P(), P())
    return jax.shard_map(
        body,
        mesh=mesh,
        in_specs=placed,
        out_specs=P("row", None, "col", None, None),
        check_vma=False,
    )
```

```python
import jax
import jax.numpy as jnp
from jax import lax
from jax.sharding import PartitionSpec as P
from jax.experimental import pallas as pl
from jax.experimental.pallas import tpu as pltpu

HI = lax.Precision.HIGHEST


def mm(a, b, precision=HI):
    return lax.dot_general(
        a, b, (((1,), (1,)), ((), ())), precision=precision, preferred_element_type=jnp.float32
    )


def kernel_tile(xrow, xcol, weights):
    weighted = xrow * weights
    sq_row = jnp.sum(weighted * xrow, axis=1)
    sq_col = jnp.sum(xcol * xcol * weights, axis=1)
    cross = mm(weighted, xcol, lax.Precision.HIGH)
    dist_sq = jnp.maximum(sq_row[:, None] + sq_col[None, :] - 2.0 * cross, 0.0)
    dist = jnp.sqrt(3.0 * dist_sq)
    return (1.0 + dist) * jnp.exp(-dist)


BASE = 128
PHASE = 16
NPIV = 4


def _chol_base_kernel(a_ref, l_ref, m_ref, w_ref):
    n = a_ref.shape[0]
    w_ref[...] = a_ref[...]
    rows = lax.broadcasted_iota(jnp.int32, (n, n), 0)
    lanes = lax.broadcasted_iota(jnp.int32, (n, n), 1)
    m_ref[...] = jnp.where(rows == lanes, 1.0, 0.0).astype(jnp.float32)
    lane1 = lax.broadcasted_iota(jnp.int32, (1, n), 1)
    for q in range(n // PHASE):
        lo = q * PHASE
        size = n - lo
        sub_rows = lax.broadcasted_iota(jnp.int32, (size, 1), 0) + lo
        sub_lanes = lax.broadcasted_iota(jnp.int32, (size, n), 1)

        def step(i, carry, lo=lo, size=size, sub_rows=sub_rows, sub_lanes=sub_lanes):
            j = lo + NPIV * i
            r = [w_ref[pl.ds(j + t, 1), :] for t in range(NPIV)]
            blk = [
                [jnp.sum(jnp.where(lane1 == j + u, r[t], 0.0), axis=1, keepdims=True) for u in range(t + 1)]
                for t in range(NPIV)
            ]
            w = w_ref[pl.ds(lo, size), :]
            wc = [
                jnp.sum(jnp.where(sub_lanes == j + t, w, 0.0), axis=1, keepdims=True)
                for t in range(NPIV)
            ]
            low = [[None] * NPIV for _ in range(NPIV)]
            rs = [None] * NPIV
            for t in range(NPIV):
                for u in range(t):
                    acc = blk[t][u]
                    for v in range(u):
                        acc = acc - low[t][v] * low[u][v]
                    low[t][u] = acc * rs[u]
                acc = blk[t][t]
                for v in range(t):
                    acc = acc - low[t][v] * low[t][v]
                rs[t] = lax.rsqrt(acc)
            below = sub_rows > j + NPIV - 1
            urow, crow, grow = [], [], []
            for t in range(NPIV):
                ut, ct = r[t], wc[t]
                gt = m_ref[pl.ds(j + t, 1), :]
                for v in range(t):
                    ut = ut - low[t][v] * urow[v]
                    ct = ct - crow[v] * low[t][v]
                    gt = gt - low[t][v] * grow[v]
                urow.append(jnp.where(lane1 >= j + t, ut * rs[t], 0.0))
                crow.append(ct * rs[t])
                grow.append(gt * rs[t])
            crow = [jnp.where(below, ct, 0.0) for ct in crow]
            g = m_ref[pl.ds(lo, size), :]
            for t in range(NPIV):
                w = w - crow[t] * urow[t]
                g = g - crow[t] * grow[t]
            w_ref[pl.ds(lo, size), :] = w
            m_ref[pl.ds(lo, size), :] = g
            for t in range(NPIV):
                w_ref[pl.ds(j + t, 1), :] = urow[t]
                m_ref[pl.ds(j + t, 1), :] = grow[t]
            return carry

        lax.fori_loop(0, PHASE // NPIV, step, 0)
    lt = jnp.where(lanes >= rows, w_ref[...], 0.0)
    l_ref[...] = lt.T
    m_ref[...] = jnp.where(rows >= lanes, m_ref[...], 0.0)


def chol_base(a):
    n = a.shape[0]
    return pl.pallas_call(
        _chol_base_kernel,
        out_shape=(
            jax.ShapeDtypeStruct((n, n), jnp.float32),
            jax.ShapeDtypeStruct((n, n), jnp.float32),
        ),
        scratch_shapes=[pltpu.VMEM((n, n), jnp.float32)],
    )(a)


def dot(a, b):
    return jnp.dot(a, b, precision=HI, preferred_element_type=jnp.float32)


def chol_inv(a):
    n = a.shape[0]
    if n <= BASE:
        return chol_base(a)
    h = n // 2
    l11, m11 = chol_inv(a[:h, :h])
    l21 = mm(a[h:, :h], m11)
    l22, m22 = chol_inv(a[h:, h:] - mm(l21, l21))
    m21 = -dot(dot(m22, l21), m11)
    zero = jnp.zeros((h, n - h), jnp.float32)
    low = jnp.concatenate([jnp.concatenate([l11, zero], 1), jnp.concatenate([l21, l22], 1)], 0)
    inv = jnp.concatenate([jnp.concatenate([m11, zero], 1), jnp.concatenate([m21, m22], 1)], 0)
    return low, inv


def body(points, nugget, weights, band_start):
    n_row = lax.axis_size("row")
    n_col = lax.axis_size("col")
    blocks = n_row // n_col
    tile, cov = points.shape
    piece = tile // n_row
    my_row = lax.axis_index("row")
    my_col = lax.axis_index("col")

    flat = points.reshape(n_row, piece * cov)
    nug_pad = jnp.pad(nugget.reshape(n_row, piece), ((0, 0), (0, 128 - piece)))
    recv = lax.all_to_all(jnp.concatenate([flat, nug_pad], axis=1), "row", 0, 0, tiled=True)
    width = recv.shape[1]
    mine = lax.dynamic_slice_in_dim(recv.reshape(blocks, n_col, width), my_col, 1, axis=1)[:, 0]
    sel = jnp.concatenate([recv[:2], mine], axis=0)
    got = lax.all_gather(sel, "row", axis=1)
    xs = got[:, :, : piece * cov].reshape(2 + blocks, tile, cov)
    ns = got[:, :, piece * cov : piece * cov + piece].reshape(2 + blocks, tile)
    x0, x1 = xs[0], xs[1]
    xcols = xs[2:]
    n0, n1 = ns[0], ns[1]

    cols = my_col + n_col * jnp.arange(blocks, dtype=jnp.int32)
    rows = jnp.concatenate([my_row[None], cols])
    nr = len(rows)
    xr_all = jnp.concatenate([points[None], xcols], axis=0).reshape(nr * tile, cov)
    eye = jnp.eye(tile, dtype=jnp.float32)
    rmask = lambda m: m[:, None, None]

    a00 = kernel_tile(x0, x0, weights) + eye * n0[None, :]
    a10 = kernel_tile(x1, x0, weights)
    a11 = kernel_tile(x1, x1, weights) + eye * n1[None, :]

    bs = band_start[rows]
    kr0 = kernel_tile(xr_all, x0, weights).reshape(nr, tile, tile)
    ar0 = jnp.where(rmask(bs <= 0), kr0, 0.0) + jnp.where(rmask(rows == 0), eye * n0[None, :], 0.0)
    kr1 = kernel_tile(xr_all, x1, weights).reshape(nr, tile, tile)
    ar1 = jnp.where(rmask((bs <= 1) & (rows >= 1)), kr1, 0.0)
    ar1 = ar1 + jnp.where(rmask(rows == 1), eye * n1[None, :], 0.0)

    l00, m0 = chol_inv(a00)
    l01 = mm(a10, m0)
    lr0 = mm(ar0.reshape(nr * tile, tile), m0).reshape(nr, tile, tile)
    lr0 = jnp.where(rmask(rows == 0), l00[None], lr0)

    l11, m1 = chol_inv(a11 - mm(l01, l01))
    upd1 = mm(lr0.reshape(nr * tile, tile), l01, lax.Precision.HIGH).reshape(nr, tile, tile)
    ar1 = ar1 - jnp.where(rmask(rows >= 1), upd1, 0.0)
    lr1 = mm(ar1.reshape(nr * tile, tile), m1).reshape(nr, tile, tile)
    lr1 = jnp.where(rmask(rows > 1), lr1, jnp.where(rmask(rows == 1), l11[None], 0.0))

    bsr = band_start[my_row]
    out = []
    for k in range(blocks):
        col = cols[k]
        a = kernel_tile(points, xcols[k], weights)
        a = jnp.where((col >= bsr) & (col <= my_row), a, 0.0)
        a = a + jnp.where(col == my_row, eye * nugget[None, :], 0.0)
        prod = mm(lr0[0], lr0[1 + k], lax.Precision.HIGH) + mm(lr1[0], lr1[1 + k], lax.Precision.HIGH)
        res = a - jnp.where((col > 1) & (col <= my_row), prod, 0.0)
        res = jnp.where(col == 0, lr0[0], jnp.where(col == 1, lr1[0], res))
        out.append(res)
    return jnp.stack(out).reshape(1, blocks, 1, tile, tile)


def solution(mesh):
    placed = (P("row", None), P("row"), P(), P())
    return jax.shard_map(
        body,
        mesh=mesh,
        in_specs=placed,
        out_specs=P("row", None, "col", None, None),
        check_vma=False,
    )
```
